128 devices in a mesh: pr: 8 (over z, core), pc: 16 (over y, x).
Axes of the slice: x: 4, y: 4, z: 4, core: 2. Of those that a mesh axis runs over, the one named last changes fastest.
Arguments:
- test_points: bfloat16 [131072, 512], P('pr'), may hold values from -15 to 15
- panel_points: bfloat16 [1024, 512], P('pc'), may hold values from -15 to 15
- factor_rows: float32 [1024, 32768], P('pc', 'pr'), may hold values from -0.03125 to 0.03125
- alpha_below: float32 [32768, 128], P(('pr', 'pc')), may hold values from -6 to 6
- targets: float32 [1024, 128], P('pc'), may hold values from -6 to 6
- inverse_block: float32 [1024, 1024], P('pc'), may hold values from -0.008 to 0.08, as said below
- predictions_in: float32 [131072, 128], P(('pr', 'pc')), may hold values from -6 to 6
Outputs:
- predictions: float32 [131072, 128], P(('pr', 'pc'))
The draws below stay inside these ranges and needn't reach their ends.
Inputs may be any that keep to these rules, and one draw needn't show every extreme that they name: `inverse_block`: lower triangular with a positive diagonal.
All inputs are finite; a program needn't handle non-finite values.
Results may differ from the reference program's by a relative error of at most 0.0003.
Values may be sent and summed in bfloat16 or wider, within the bound.
No kernel may reach another device: no remote copies, remote signals or barrier semaphores. Data moves between devices by JAX's collectives and lax.ppermute only.
A program may use at most 128 MiB of HBM per device.

```python
import math
import jax
import jax.numpy as jnp
from jax import lax

D = 512
OUTS = 128
PANEL = 1024
LAYERS = 4
TEST_ROW = 16384
NS = 32768
TEST = 131072
N_PR = 8


def point_cloud(key, count, salt):
    centers = jnp.clip(jax.random.normal(jax.random.fold_in(key, 11), (32, D), jnp.float32), -4.0, 4.0)
    member = jax.random.randint(jax.random.fold_in(key, salt + 1), (count,), 0, 32)
    mixing = jax.random.uniform(jax.random.fold_in(key, salt + 2), (count, 1), jnp.float32, 0.2, 0.85)
    noise = jnp.clip(jax.random.normal(jax.random.fold_in(key, salt + 3), (count, D), jnp.float32), -4.0, 4.0)
    scales = jnp.exp(jax.random.uniform(jax.random.fold_in(key, salt + 4), (count, 1), jnp.float32, math.log(0.5), math.log(2.0)))
    points = scales * (jnp.sqrt(mixing) * centers[member] + jnp.sqrt(1.0 - mixing) * noise)
    return points.astype(jnp.bfloat16)


def draw_test_points(key, part):
    return point_cloud(key, TEST, 100)


def draw_panel_points(key, part):
    return point_cloud(key, PANEL, 200)


def draw_inverse_block(key, part):
    rows = jnp.arange(PANEL)[:, None]
    columns = jnp.arange(PANEL)[None, :]
    diagonal = jnp.exp(jax.random.uniform(jax.random.fold_in(key, 301), (PANEL, 1), jnp.float32, math.log(0.02), math.log(0.08)))
    lower = 0.002 * jnp.clip(jax.random.normal(jax.random.fold_in(key, 302), (PANEL, PANEL), jnp.float32), -4.0, 4.0)
    return jnp.where(rows == columns, diagonal, jnp.where(rows > columns, lower, 0.0)).astype(jnp.float32)


def shard_levels(stream_key, shape, cuts, low, largest):
    gain, own = 1.0, jax.random.fold_in(stream_key, 6)
    for dim, shards_of in cuts:
        draws = jnp.exp(jax.random.uniform(jax.random.fold_in(own, dim), (shards_of,), jnp.float32, low / len(cuts), largest / len(cuts)))
        gain = gain * jnp.repeat(draws, shape[dim] // shards_of).reshape([-1 if axis == dim else 1 for axis in range(len(shape))])
    return gain


def normal_values(stream_key, extent, deviation, reach, cuts=(), dtype=jnp.bfloat16):
    drawn = deviation * jax.random.normal(stream_key, extent, jnp.float32)
    if cuts:
        drawn = drawn * shard_levels(stream_key, extent, cuts, -0.22, 0.18)
    return jnp.clip(drawn, -reach, reach).astype(dtype)


def setup_inputs(seed: int = 0) -> dict:
    arg_keys = jax.random.split(jax.random.key(seed), 8)
    test_points = draw_test_points(jax.random.fold_in(arg_keys[7], 71), 0)
    panel_points = draw_panel_points(jax.random.fold_in(arg_keys[7], 71), 0)
    factor_rows = normal_values(arg_keys[2], (PANEL, NS), NS ** -0.5, 0.03125, ((0, 16), (1, 8)), jnp.float32)
    alpha_below = normal_values(arg_keys[3], (NS, OUTS), 1.0, 6.0, ((0, 128),), jnp.float32)
    targets = normal_values(arg_keys[4], (PANEL, OUTS), 1.0, 6.0, ((0, 16),), jnp.float32)
    inverse_block = draw_inverse_block(jax.random.fold_in(arg_keys[7], 71), 0)
    predictions_in = normal_values(arg_keys[6], (TEST, OUTS), 1.0, 6.0, ((0, 128),), jnp.float32)
    return {"test_points": test_points, "panel_points": panel_points, "factor_rows": factor_rows, "alpha_below": alpha_below, "targets": targets, "inverse_block": inverse_block, "predictions_in": predictions_in}


bias_var = 0.1
weight_var = 2.0

def arc_kernel(panel, test):
    cross = jnp.dot(panel, test.T, preferred_element_type=jnp.float32) / D
    panel_var = jnp.einsum('pd,pd->p', panel, panel, preferred_element_type=jnp.float32) / D
    test_var = jnp.einsum('nd,nd->n', test, test, preferred_element_type=jnp.float32) / D
    kern = bias_var + weight_var * cross
    panel_k = bias_var + weight_var * panel_var
    test_k = bias_var + weight_var * test_var
    for level in range(LAYERS):
        spread = jnp.sqrt(panel_k[:, None] * test_k[None, :])
        cosine = kern / spread
        theta = jnp.arccos(cosine)
        kern = bias_var + weight_var / (2.0 * math.pi) * spread * (jnp.sqrt(1.0 - cosine * cosine) + (math.pi - theta) * cosine)
        panel_k = bias_var + 0.5 * weight_var * panel_k
        test_k = bias_var + 0.5 * weight_var * test_k
    return kern

def reference(test_points, panel_points, factor_rows, alpha_below, targets, inverse_block, predictions_in):
    carried = jnp.dot(factor_rows, alpha_below, precision=lax.Precision.HIGHEST, preferred_element_type=jnp.float32)
    residual = targets - carried
    alpha_panel = jnp.dot(inverse_block.T, residual, precision=lax.Precision.HIGHEST, preferred_element_type=jnp.float32)
    blocks = test_points.reshape(N_PR, TEST_ROW, D)

    def one_block(test_block):
        kern = arc_kernel(panel_points, test_block)
        return lax.dot_general(kern, alpha_panel, (((0,), (0,)), ((), ())), precision=lax.Precision.HIGHEST, preferred_element_type=jnp.float32)
    update = lax.map(one_block, blocks).reshape(TEST, OUTS)
    return predictions_in + update
```

```python
import math

import jax
import jax.numpy as jnp
from jax import lax
from jax.sharding import PartitionSpec as P

LAYERS = 4


bias_var = 0.1
weight_var = 2.0


def arc_kernel(panel, test, test_norms):
    width = panel.shape[1]
    cross = jnp.dot(panel, test.T, preferred_element_type=jnp.float32) / width
    panel_var = jnp.einsum("pd,pd->p", panel, panel, preferred_element_type=jnp.float32) / width
    kern = bias_var + weight_var * cross
    panel_k = bias_var + weight_var * panel_var
    test_k = bias_var + weight_var * (test_norms / width)
    for level in range(LAYERS):
        spread = jnp.sqrt(panel_k[:, None] * test_k[None, :])
        cosine = kern / spread
        theta = jnp.arccos(cosine)
        kern = bias_var + weight_var / (2.0 * math.pi) * spread * (
            jnp.sqrt(1.0 - cosine * cosine) + (math.pi - theta) * cosine
        )
        panel_k = bias_var + 0.5 * weight_var * panel_k
        test_k = bias_var + 0.5 * weight_var * test_k
    return kern


def contract_rows(left, right):
    return lax.dot_general(
        left,
        right,
        (((0,), (0,)), ((), ())),
        precision=lax.Precision.HIGHEST,
        preferred_element_type=jnp.float32,
    )


def body(
    test_points, panel_points, factor_rows, alpha_below, targets, inverse_block, predictions_in
):
    rows = predictions_in.shape[0]
    own = lax.axis_index("pc")
    partial_sum = jnp.dot(
        factor_rows,
        lax.all_gather(alpha_below, "pc", axis=0, tiled=True),
        precision=lax.Precision.HIGHEST,
        preferred_element_type=jnp.float32,
    )
    carried = lax.psum(partial_sum, "pr")
    residual = targets - carried
    alpha_panel = lax.psum(contract_rows(inverse_block, residual), "pc")
    panel_all = lax.all_gather(panel_points, "pc", axis=0, tiled=True)
    test_own = lax.dynamic_slice_in_dim(test_points, own * rows, rows, 0)
    test_norms = jnp.einsum(
        "nd,nd->n", test_own, test_own, preferred_element_type=jnp.float32
    )
    kern = lax.optimization_barrier(arc_kernel(panel_all, test_own, test_norms))
    update = contract_rows(kern, alpha_panel)
    return predictions_in + update


def solution(mesh):
    placed = (
        P("pr", None),
        P("pc", None),
        P("pc", "pr"),
        P(("pr", "pc"), None),
        P("pc", None),
        P("pc", None),
        P(("pr", "pc"), None),
    )
    return jax.shard_map(
        body, mesh=mesh, in_specs=placed, out_specs=P(("pr", "pc"), None), check_vma=False
    )
```

```python
import math

import jax
import jax.numpy as jnp
from jax import lax
from jax.sharding import PartitionSpec as P

LAYERS = 4


bias_var = 0.1
weight_var = 2.0


def arc_kernel(panel, test, test_norms):
    width = panel.shape[1]
    cross = jnp.dot(panel, test.T, preferred_element_type=jnp.float32) / width
    panel_var = jnp.einsum("pd,pd->p", panel, panel, preferred_element_type=jnp.float32) / width
    kern = bias_var + weight_var * cross
    panel_k = bias_var + weight_var * panel_var
    test_k = bias_var + weight_var * (test_norms / width)
    for level in range(LAYERS):
        spread = jnp.sqrt(panel_k[:, None] * test_k[None, :])
        cosine = kern / spread
        theta = jnp.arccos(cosine)
        kern = bias_var + weight_var / (2.0 * math.pi) * spread * (
            jnp.sqrt(1.0 - cosine * cosine) + (math.pi - theta) * cosine
        )
        panel_k = bias_var + 0.5 * weight_var * panel_k
        test_k = bias_var + 0.5 * weight_var * test_k
    return kern


def contract_rows(left, right):
    return lax.dot_general(
        left,
        right,
        (((0,), (0,)), ((), ())),
        precision=lax.Precision.HIGHEST,
        preferred_element_type=jnp.float32,
    )


def gather_rows(x, axis, n):
    copies = jnp.broadcast_to(x[None], (n,) + x.shape)
    return lax.all_to_all(copies, axis, 0, 0, tiled=False).reshape((-1,) + x.shape[1:])


def sum_rows(x, axis, n):
    blocks = lax.all_to_all(x.reshape((n, -1) + x.shape[1:]), axis, 0, 0, tiled=False)
    return gather_rows(blocks.sum(0), axis, n)


def butterfly_sum(x, axis, n):
    step = 1
    while step < n:
        x = x + lax.ppermute(x, axis, [(i, i ^ step) for i in range(n)])
        step *= 2
    return x


def body(
    test_points, panel_points, factor_rows, alpha_below, targets, inverse_block, predictions_in
):
    n_pr = lax.axis_size("pr")
    n_pc = lax.axis_size("pc")
    rows = predictions_in.shape[0]
    own = lax.axis_index("pc")
    panel_all = lax.all_gather(panel_points, "pc", axis=0, tiled=True)
    partial_sum = jnp.dot(
        factor_rows,
        gather_rows(alpha_below, "pc", n_pc),
        precision=lax.Precision.HIGHEST,
        preferred_element_type=jnp.float32,
    )
    carried = butterfly_sum(partial_sum, "pr", n_pr)
    residual = targets - carried
    alpha_panel = sum_rows(contract_rows(inverse_block, residual), "pc", n_pc)
    test_own = lax.dynamic_slice_in_dim(test_points, own * rows, rows, 0)
    test_norms = jnp.einsum(
        "nd,nd->n", test_own, test_own, preferred_element_type=jnp.float32
    )
    kern = lax.optimization_barrier(arc_kernel(panel_all, test_own, test_norms))
    update = contract_rows(kern, alpha_panel)
    return predictions_in + update


def solution(mesh):
    placed = (
        P("pr", None),
        P("pc", None),
        P("pc", "pr"),
        P(("pr", "pc"), None),
        P("pc", None),
        P("pc", None),
        P(("pr", "pc"), None),
    )
    return jax.shard_map(
        body, mesh=mesh, in_specs=placed, out_specs=P(("pr", "pc"), None), check_vma=False
    )
```

```python
import math

import jax
import jax.numpy as jnp
from jax import lax
from jax.sharding import PartitionSpec as P

LAYERS = 4


bias_var = 0.1
weight_var = 2.0


ASIN_COEFFS = (4.2163199048e-2, 2.4181311049e-2, 4.5470025998e-2, 7.4953002686e-2, 1.6666752422e-1)


def reflected_arccos(cosine):
    size = jnp.abs(cosine)
    big = size > 0.5
    z = jnp.where(big, 0.5 - 0.5 * size, size * size)
    x = jnp.where(big, jnp.sqrt(z), size)
    poly = ASIN_COEFFS[0]
    for coeff in ASIN_COEFFS[1:]:
        poly = poly * z + coeff
    arcsine = x + x * z * poly
    arccos_size = jnp.where(big, 2.0 * arcsine, 0.5 * math.pi - arcsine)
    return jnp.where(cosine >= 0.0, math.pi - arccos_size, arccos_size)


def arc_kernel(panel, test, test_norms):
    width = panel.shape[1]
    cross = jnp.dot(panel, test.T, preferred_element_type=jnp.float32) / width
    panel_var = jnp.einsum("pd,pd->p", panel, panel, preferred_element_type=jnp.float32) / width
    kern = bias_var + weight_var * cross
    panel_k = bias_var + weight_var * panel_var
    test_k = bias_var + weight_var * (test_norms / width)
    for level in range(LAYERS):
        panel_root = jnp.sqrt(panel_k)
        test_root = jnp.sqrt(test_k)
        spread = panel_root[:, None] * test_root[None, :]
        inverse = (1.0 / panel_root)[:, None] * (1.0 / test_root)[None, :]
        cosine = jnp.clip(kern * inverse, -1.0, 1.0)
        kern = bias_var + weight_var / (2.0 * math.pi) * (
            spread * jnp.sqrt(1.0 - cosine * cosine) + reflected_arccos(cosine) * kern
        )
        panel_k = bias_var + 0.5 * weight_var * panel_k
        test_k = bias_var + 0.5 * weight_var * test_k
    return kern


def contract_rows(left, right):
    return lax.dot_general(
        left,
        right,
        (((0,), (0,)), ((), ())),
        precision=lax.Precision.HIGHEST,
        preferred_element_type=jnp.float32,
    )


def gather_rows(x, axis, n):
    copies = jnp.broadcast_to(x[None], (n,) + x.shape)
    return lax.all_to_all(copies, axis, 0, 0, tiled=False).reshape((-1,) + x.shape[1:])


def sum_rows(x, axis, n):
    blocks = lax.all_to_all(x.reshape((n, -1) + x.shape[1:]), axis, 0, 0, tiled=False)
    return gather_rows(blocks.sum(0), axis, n)


def butterfly_sum(x, axis, n):
    step = 1
    while step < n:
        x = x + lax.ppermute(x, axis, [(i, i ^ step) for i in range(n)])
        step *= 2
    return x


def body(
    test_points, panel_points, factor_rows, alpha_below, targets, inverse_block, predictions_in
):
    n_pr = lax.axis_size("pr")
    n_pc = lax.axis_size("pc")
    rows = predictions_in.shape[0]
    own = lax.axis_index("pc")
    panel_all = lax.all_gather(panel_points, "pc", axis=0, tiled=True)
    partial_sum = jnp.dot(
        factor_rows,
        gather_rows(alpha_below, "pc", n_pc),
        precision=lax.Precision.HIGHEST,
        preferred_element_type=jnp.float32,
    )
    carried = butterfly_sum(partial_sum, "pr", n_pr)
    residual = targets - carried
    alpha_panel = sum_rows(contract_rows(inverse_block, residual), "pc", n_pc)
    test_own = lax.dynamic_slice_in_dim(test_points, own * rows, rows, 0)
    test_norms = jnp.einsum(
        "nd,nd->n", test_own, test_own, preferred_element_type=jnp.float32
    )
    kern = lax.optimization_barrier(arc_kernel(panel_all, test_own, test_norms))
    update = contract_rows(kern, alpha_panel)
    return predictions_in + update


def solution(mesh):
    placed = (
        P("pr", None),
        P("pc", None),
        P("pc", "pr"),
        P(("pr", "pc"), None),
        P("pc", None),
        P("pc", None),
        P(("pr", "pc"), None),
    )
    return jax.shard_map(
        body, mesh=mesh, in_specs=placed, out_specs=P(("pr", "pc"), None), check_vma=False
    )
```

```python
import math

import jax
import jax.numpy as jnp
from jax import lax
from jax.sharding import PartitionSpec as P

LAYERS = 4


bias_var = 0.1
weight_var = 2.0


ASIN_COEFFS = (4.2163199048e-2, 2.4181311049e-2, 4.5470025998e-2, 7.4953002686e-2, 1.6666752422e-1)


def reflected_arccos(cosine):
    size = jnp.abs(cosine)
    big = size > 0.5
    z = jnp.where(big, 0.5 - 0.5 * size, size * size)
    x = jnp.where(big, jnp.sqrt(z), size)
    poly = ASIN_COEFFS[0]
    for coeff in ASIN_COEFFS[1:]:
        poly = poly * z + coeff
    arcsine = x + x * z * poly
    arccos_size = jnp.where(big, 2.0 * arcsine, 0.5 * math.pi - arcsine)
    return jnp.where(cosine >= 0.0, math.pi - arccos_size, arccos_size)


def arc_kernel(panel, test, test_norms):
    width = panel.shape[1]
    cross = jnp.dot(panel, test.T, preferred_element_type=jnp.float32) / width
    panel_var = jnp.einsum("pd,pd->p", panel, panel, preferred_element_type=jnp.float32) / width
    kern = bias_var + weight_var * cross
    panel_k = bias_var + weight_var * panel_var
    test_k = bias_var + weight_var * (test_norms / width)
    for level in range(LAYERS):
        panel_root = jnp.sqrt(panel_k)
        test_root = jnp.sqrt(test_k)
        spread = panel_root[:, None] * test_root[None, :]
        inverse = (1.0 / panel_root)[:, None] * (1.0 / test_root)[None, :]
        cosine = jnp.clip(kern * inverse, -1.0, 1.0)
        kern = bias_var + weight_var / (2.0 * math.pi) * (
            spread * jnp.sqrt(1.0 - cosine * cosine) + reflected_arccos(cosine) * kern
        )
        panel_k = bias_var + 0.5 * weight_var * panel_k
        test_k = bias_var + 0.5 * weight_var * test_k
    return kern


def contract_rows(left, right):
    return lax.dot_general(
        left,
        right,
        (((0,), (0,)), ((), ())),
        precision=lax.Precision.HIGHEST,
        preferred_element_type=jnp.float32,
    )


def gather_rows(x, axis, n):
    copies = jnp.broadcast_to(x[None], (n,) + x.shape)
    return lax.all_to_all(copies, axis, 0, 0, tiled=False).reshape((-1,) + x.shape[1:])


def sum_rows(x, axis, n):
    blocks = lax.all_to_all(x.reshape((n, -1) + x.shape[1:]), axis, 0, 0, tiled=False)
    return gather_rows(blocks.sum(0), axis, n)


def butterfly_sum(x, axis, n):
    step = 1
    while step < n:
        x = x + lax.ppermute(x, axis, [(i, i ^ step) for i in range(n)])
        step *= 2
    return x


def body(
    test_points, panel_points, factor_rows, alpha_below, targets, inverse_block, predictions_in
):
    n_pr = lax.axis_size("pr")
    n_pc = lax.axis_size("pc")
    rows = predictions_in.shape[0]
    own = lax.axis_index("pc")
    panel_all = gather_rows(panel_points, "pc", n_pc)
    test_own = lax.dynamic_slice_in_dim(test_points, own * rows, rows, 0)
    test_norms = jnp.einsum(
        "nd,nd->n", test_own, test_own, preferred_element_type=jnp.float32
    )
    kern = arc_kernel(panel_all, test_own, test_norms)
    gathered = gather_rows(alpha_below, "pc", n_pc)
    kern, gathered = lax.optimization_barrier((kern, gathered))
    partial_sum = jnp.dot(
        factor_rows,
        gathered,
        precision=lax.Precision.HIGHEST,
        preferred_element_type=jnp.float32,
    )
    carried = butterfly_sum(partial_sum, "pr", n_pr)
    residual = targets - carried
    alpha_panel = sum_rows(contract_rows(inverse_block, residual), "pc", n_pc)
    update = contract_rows(kern, alpha_panel)
    return predictions_in + update


def solution(mesh):
    placed = (
        P("pr", None),
        P("pc", None),
        P("pc", "pr"),
        P(("pr", "pc"), None),
        P("pc", None),
        P("pc", None),
        P(("pr", "pc"), None),
    )
    return jax.shard_map(
        body, mesh=mesh, in_specs=placed, out_specs=P(("pr", "pc"), None), check_vma=False
    )
```

```python
import math

import jax
import jax.numpy as jnp
from jax import lax
from jax.sharding import PartitionSpec as P

LAYERS = 4


bias_var = 0.1
weight_var = 2.0


ASIN_COEFFS = (4.2163199048e-2, 2.4181311049e-2, 4.5470025998e-2, 7.4953002686e-2, 1.6666752422e-1)


def reflected_arccos(cosine):
    size = jnp.abs(cosine)
    big = size > 0.5
    z = jnp.where(big, 0.5 - 0.5 * size, size * size)
    x = jnp.where(big, jnp.sqrt(z), size)
    poly = ASIN_COEFFS[0]
    for coeff in ASIN_COEFFS[1:]:
        poly = poly * z + coeff
    arcsine = x + x * z * poly
    arccos_size = jnp.where(big, 2.0 * arcsine, 0.5 * math.pi - arcsine)
    return jnp.where(cosine >= 0.0, math.pi - arccos_size, arccos_size)


def arc_kernel(panel, test, test_norms):
    width = panel.shape[1]
    cross = jnp.dot(panel, test.T, preferred_element_type=jnp.float32) / width
    panel_var = jnp.einsum("pd,pd->p", panel, panel, preferred_element_type=jnp.float32) / width
    kern = bias_var + weight_var * cross
    panel_k = bias_var + weight_var * panel_var
    test_k = bias_var + weight_var * (test_norms / width)
    for level in range(LAYERS):
        panel_root = jnp.sqrt(panel_k)
        test_root = jnp.sqrt(test_k)
        spread = panel_root[:, None] * test_root[None, :]
        inverse = (1.0 / panel_root)[:, None] * (1.0 / test_root)[None, :]
        cosine = jnp.clip(kern * inverse, -1.0, 1.0)
        kern = bias_var + weight_var / (2.0 * math.pi) * (
            spread * jnp.sqrt(1.0 - cosine * cosine) + reflected_arccos(cosine) * kern
        )
        panel_k = bias_var + 0.5 * weight_var * panel_k
        test_k = bias_var + 0.5 * weight_var * test_k
    return kern


def contract_rows(left, right):
    return lax.dot_general(
        left,
        right,
        (((0,), (0,)), ((), ())),
        precision=lax.Precision.HIGHEST,
        preferred_element_type=jnp.float32,
    )


def gather_rows(x, axis, n):
    copies = jnp.broadcast_to(x[None], (n,) + x.shape)
    return lax.all_to_all(copies, axis, 0, 0, tiled=False).reshape((-1,) + x.shape[1:])


def sum_rows(x, axis, n):
    blocks = lax.all_to_all(x.reshape((n, -1) + x.shape[1:]), axis, 0, 0, tiled=False)
    return gather_rows(blocks.sum(0), axis, n)


def butterfly_sum(x, axis, n):
    step = 1
    while step < n:
        x = x + lax.ppermute(x, axis, [(i, i ^ step) for i in range(n)])
        step *= 2
    return x


def body(
    test_points, panel_points, factor_rows, alpha_below, targets, inverse_block, predictions_in
):
    n_pr = lax.axis_size("pr")
    n_pc = lax.axis_size("pc")
    rows = predictions_in.shape[0]
    own = lax.axis_index("pc")
    gathered = gather_rows(alpha_below, "pc", n_pc)
    panel_all = lax.all_gather(panel_points, "pc", axis=0, tiled=True)
    test_own = lax.dynamic_slice_in_dim(test_points, own * rows, rows, 0)
    test_norms = jnp.einsum(
        "nd,nd->n", test_own, test_own, preferred_element_type=jnp.float32
    )
    partial_sum = jnp.dot(
        factor_rows,
        gathered,
        precision=lax.Precision.HIGHEST,
        preferred_element_type=jnp.float32,
    )
    carried = butterfly_sum(partial_sum, "pr", n_pr)
    residual = targets - carried
    spread_alpha = contract_rows(inverse_block, residual)
    spread_alpha, panel_all = lax.optimization_barrier((spread_alpha, panel_all))
    half = rows // 2
    blocks = lax.all_to_all(
        spread_alpha.reshape((n_pc, -1) + spread_alpha.shape[1:]), "pc", 0, 0, tiled=False
    )
    kern_a = arc_kernel(panel_all, test_own[:half], test_norms[:half])
    kern_a, blocks = lax.optimization_barrier((kern_a, blocks))
    own_block = blocks.sum(0)
    own_block, panel_all = lax.optimization_barrier((own_block, panel_all))
    alpha_panel = gather_rows(own_block, "pc", n_pc)
    kern_b = arc_kernel(panel_all, test_own[half:], test_norms[half:])
    kern_b, alpha_panel = lax.optimization_barrier((kern_b, alpha_panel))
    update = jnp.concatenate(
        [contract_rows(kern_a, alpha_panel), contract_rows(kern_b, alpha_panel)]
    )
    return predictions_in + update


def solution(mesh):
    placed = (
        P("pr", None),
        P("pc", None),
        P("pc", "pr"),
        P(("pr", "pc"), None),
        P("pc", None),
        P("pc", None),
        P(("pr", "pc"), None),
    )
    return jax.shard_map(
        body, mesh=mesh, in_specs=placed, out_specs=P(("pr", "pc"), None), check_vma=False
    )
```

```python
import math

import jax
import jax.numpy as jnp
from jax import lax
from jax.sharding import PartitionSpec as P

LAYERS = 4


bias_var = 0.1
weight_var = 2.0


ASIN_COEFFS = (4.2163199048e-2, 2.4181311049e-2, 4.5470025998e-2, 7.4953002686e-2, 1.6666752422e-1)


def reflected_arccos(cosine):
    size = jnp.abs(cosine)
    big = size > 0.5
    z = jnp.where(big, 0.5 - 0.5 * size, size * size)
    x = jnp.where(big, jnp.sqrt(z), size)
    poly = ASIN_COEFFS[0]
    for coeff in ASIN_COEFFS[1:]:
        poly = poly * z + coeff
    arcsine = x + x * z * poly
    arccos_size = jnp.where(big, 2.0 * arcsine, 0.5 * math.pi - arcsine)
    return jnp.where(cosine >= 0.0, math.pi - arccos_size, arccos_size)


def arc_kernel(panel, test, test_norms):
    width = panel.shape[1]
    cross = jnp.dot(panel, test.T, preferred_element_type=jnp.float32) / width
    panel_var = jnp.einsum("pd,pd->p", panel, panel, preferred_element_type=jnp.float32) / width
    kern = bias_var + weight_var * cross
    panel_k = bias_var + weight_var * panel_var
    test_k = bias_var + weight_var * (test_norms / width)
    for level in range(LAYERS):
        panel_root = jnp.sqrt(panel_k)
        test_root = jnp.sqrt(test_k)
        spread = panel_root[:, None] * test_root[None, :]
        inverse = (1.0 / panel_root)[:, None] * (1.0 / test_root)[None, :]
        cosine = jnp.clip(kern * inverse, -1.0, 1.0)
        kern = bias_var + weight_var / (2.0 * math.pi) * (
            spread * jnp.sqrt(1.0 - cosine * cosine) + reflected_arccos(cosine) * kern
        )
        panel_k = bias_var + 0.5 * weight_var * panel_k
        test_k = bias_var + 0.5 * weight_var * test_k
    return kern


def contract_rows(left, right):
    return lax.dot_general(
        left,
        right,
        (((0,), (0,)), ((), ())),
        precision=lax.Precision.HIGHEST,
        preferred_element_type=jnp.float32,
    )


def gather_rows(x, axis, n):
    copies = jnp.broadcast_to(x[None], (n,) + x.shape)
    return lax.all_to_all(copies, axis, 0, 0, tiled=False).reshape((-1,) + x.shape[1:])


def sum_rows(x, axis, n):
    blocks = lax.all_to_all(x.reshape((n, -1) + x.shape[1:]), axis, 0, 0, tiled=False)
    return gather_rows(blocks.sum(0), axis, n)


def butterfly_sum(x, axis, n):
    step = 1
    while step < n:
        x = x + lax.ppermute(x, axis, [(i, i ^ step) for i in range(n)])
        step *= 2
    return x


def body(
    test_points, panel_points, factor_rows, alpha_below, targets, inverse_block, predictions_in
):
    n_pr = lax.axis_size("pr")
    n_pc = lax.axis_size("pc")
    rows = predictions_in.shape[0]
    own = lax.axis_index("pc")
    panel_all = gather_rows(panel_points, "pc", n_pc)
    test_own = lax.dynamic_slice_in_dim(test_points, own * rows, rows, 0)
    test_norms = jnp.einsum(
        "nd,nd->n", test_own, test_own, preferred_element_type=jnp.float32
    )
    kern = arc_kernel(panel_all, test_own, test_norms)
    gathered = lax.all_gather(alpha_below, "pc", axis=0, tiled=True)
    kern, gathered = lax.optimization_barrier((kern, gathered))
    partial_sum = jnp.dot(
        factor_rows,
        gathered,
        precision=lax.Precision.HIGHEST,
        preferred_element_type=jnp.float32,
    )
    carried = butterfly_sum(partial_sum, "pr", n_pr)
    residual = targets - carried
    alpha_panel = sum_rows(contract_rows(inverse_block, residual), "pc", n_pc)
    update = contract_rows(kern, alpha_panel)
    return predictions_in + update


def solution(mesh):
    placed = (
        P("pr", None),
        P("pc", None),
        P("pc", "pr"),
        P(("pr", "pc"), None),
        P("pc", None),
        P("pc", None),
        P(("pr", "pc"), None),
    )
    return jax.shard_map(
        body, mesh=mesh, in_specs=placed, out_specs=P(("pr", "pc"), None), check_vma=False
    )
```

```python
import math

import jax
import jax.numpy as jnp
from jax import lax
from jax.sharding import PartitionSpec as P

LAYERS = 4


bias_var = 0.1
weight_var = 2.0


ASIN_COEFFS = (4.2163199048e-2, 2.4181311049e-2, 4.5470025998e-2, 7.4953002686e-2, 1.6666752422e-1)


def reflected_arccos(cosine):
    size = jnp.abs(cosine)
    big = size > 0.5
    z = jnp.where(big, 0.5 - 0.5 * size, size * size)
    x = jnp.where(big, jnp.sqrt(z), size)
    poly = ASIN_COEFFS[0]
    for coeff in ASIN_COEFFS[1:]:
        poly = poly * z + coeff
    arcsine = x + x * z * poly
    arccos_size = jnp.where(big, 2.0 * arcsine, 0.5 * math.pi - arcsine)
    return jnp.where(cosine >= 0.0, math.pi - arccos_size, arccos_size)


def arc_kernel(panel, test, test_norms):
    width = panel.shape[1]
    cross = jnp.dot(panel, test.T, preferred_element_type=jnp.float32) / width
    panel_var = jnp.einsum("pd,pd->p", panel, panel, preferred_element_type=jnp.float32) / width
    kern = bias_var + weight_var * cross
    panel_k = bias_var + weight_var * panel_var
    test_k = bias_var + weight_var * (test_norms / width)
    for level in range(LAYERS):
        panel_root = jnp.sqrt(panel_k)
        test_root = jnp.sqrt(test_k)
        spread = panel_root[:, None] * test_root[None, :]
        inverse = (1.0 / panel_root)[:, None] * (1.0 / test_root)[None, :]
        cosine = jnp.clip(kern * inverse, -1.0, 1.0)
        kern = bias_var + weight_var / (2.0 * math.pi) * (
            spread * jnp.sqrt(1.0 - cosine * cosine) + reflected_arccos(cosine) * kern
        )
        panel_k = bias_var + 0.5 * weight_var * panel_k
        test_k = bias_var + 0.5 * weight_var * test_k
    return kern


def contract_rows(left, right):
    return lax.dot_general(
        left,
        right,
        (((0,), (0,)), ((), ())),
        precision=lax.Precision.HIGH,
        preferred_element_type=jnp.float32,
    )


def gather_rows(x, axis, n):
    copies = jnp.broadcast_to(x[None], (n,) + x.shape)
    return lax.all_to_all(copies, axis, 0, 0, tiled=False).reshape((-1,) + x.shape[1:])


def sum_rows(x, axis, n):
    blocks = lax.all_to_all(x.reshape((n, -1) + x.shape[1:]), axis, 0, 0, tiled=False)
    return gather_rows(blocks.sum(0), axis, n)


def butterfly_sum(x, axis, n):
    step = 1
    while step < n:
        x = x + lax.ppermute(x, axis, [(i, i ^ step) for i in range(n)])
        step *= 2
    return x


def body(
    test_points, panel_points, factor_rows, alpha_below, targets, inverse_block, predictions_in
):
    n_pr = lax.axis_size("pr")
    n_pc = lax.axis_size("pc")
    rows = predictions_in.shape[0]
    own = lax.axis_index("pc")
    panel_all = gather_rows(panel_points, "pc", n_pc)
    test_own = lax.dynamic_slice_in_dim(test_points, own * rows, rows, 0)
    test_norms = jnp.einsum(
        "nd,nd->n", test_own, test_own, preferred_element_type=jnp.float32
    )
    kern = arc_kernel(panel_all, test_own, test_norms)
    gathered = gather_rows(alpha_below, "pc", n_pc)
    kern, gathered = lax.optimization_barrier((kern, gathered))
    partial_sum = jnp.dot(
        factor_rows,
        gathered,
        precision=lax.Precision.HIGH,
        preferred_element_type=jnp.float32,
    )
    carried = butterfly_sum(partial_sum, "pr", n_pr)
    residual = targets - carried
    alpha_panel = sum_rows(contract_rows(inverse_block, residual), "pc", n_pc)
    update = contract_rows(kern, alpha_panel)
    return predictions_in + update


def solution(mesh):
    placed = (
        P("pr", None),
        P("pc", None),
        P("pc", "pr"),
        P(("pr", "pc"), None),
        P("pc", None),
        P("pc", None),
        P(("pr", "pc"), None),
    )
    return jax.shard_map(
        body, mesh=mesh, in_specs=placed, out_specs=P(("pr", "pc"), None), check_vma=False
    )
```

```python
import math

import jax
import jax.numpy as jnp
from jax import lax
from jax.sharding import PartitionSpec as P

LAYERS = 4


bias_var = 0.1
weight_var = 2.0


ASIN_COEFFS = (4.2163199048e-2, 2.4181311049e-2, 4.5470025998e-2, 7.4953002686e-2, 1.6666752422e-1)


def reflected_arccos(cosine):
    size = jnp.abs(cosine)
    big = size > 0.5
    z = jnp.where(big, 0.5 - 0.5 * size, size * size)
    x = jnp.where(big, jnp.sqrt(z), size)
    poly = ASIN_COEFFS[0]
    for coeff in ASIN_COEFFS[1:]:
        poly = poly * z + coeff
    arcsine = x + x * z * poly
    arccos_size = jnp.where(big, 2.0 * arcsine, 0.5 * math.pi - arcsine)
    return jnp.where(cosine >= 0.0, math.pi - arccos_size, arccos_size)


def arc_kernel(panel, test, test_norms):
    width = panel.shape[1]
    cross = jnp.dot(panel, test.T, preferred_element_type=jnp.float32) / width
    panel_var = jnp.einsum("pd,pd->p", panel, panel, preferred_element_type=jnp.float32) / width
    kern = bias_var + weight_var * cross
    panel_k = bias_var + weight_var * panel_var
    test_k = bias_var + weight_var * (test_norms / width)
    for level in range(LAYERS):
        panel_root = jnp.sqrt(panel_k)
        test_root = jnp.sqrt(test_k)
        spread = panel_root[:, None] * test_root[None, :]
        inverse = (1.0 / panel_root)[:, None] * (1.0 / test_root)[None, :]
        cosine = jnp.clip(kern * inverse, -1.0, 1.0)
        kern = bias_var + weight_var / (2.0 * math.pi) * (
            spread * jnp.sqrt(1.0 - cosine * cosine) + reflected_arccos(cosine) * kern
        )
        panel_k = bias_var + 0.5 * weight_var * panel_k
        test_k = bias_var + 0.5 * weight_var * test_k
    return kern


def contract_rows(left, right):
    return lax.dot_general(
        left,
        right,
        (((0,), (0,)), ((), ())),
        precision=lax.Precision.HIGH,
        preferred_element_type=jnp.float32,
    )


def gather_rows(x, axis, n):
    copies = jnp.broadcast_to(x[None], (n,) + x.shape)
    return lax.all_to_all(copies, axis, 0, 0, tiled=False).reshape((-1,) + x.shape[1:])


def sum_rows(x, axis, n):
    blocks = lax.all_to_all(x.reshape((n, -1) + x.shape[1:]), axis, 0, 0, tiled=False)
    return gather_rows(blocks.sum(0), axis, n)


def butterfly_sum(x, axis, n):
    step = 1
    while step < n:
        x = x + lax.ppermute(x, axis, [(i, i ^ step) for i in range(n)])
        step *= 2
    return x


def body(
    test_points, panel_points, factor_rows, alpha_below, targets, inverse_block, predictions_in
):
    n_pr = lax.axis_size("pr")
    n_pc = lax.axis_size("pc")
    rows = predictions_in.shape[0]
    own = lax.axis_index("pc")
    inverse_full = lax.all_gather(inverse_block, "pc", axis=0, tiled=True)
    panel_all = gather_rows(panel_points, "pc", n_pc)
    test_own = lax.dynamic_slice_in_dim(test_points, own * rows, rows, 0)
    test_norms = jnp.einsum(
        "nd,nd->n", test_own, test_own, preferred_element_type=jnp.float32
    )
    kern = arc_kernel(panel_all, test_own, test_norms)
    gathered = gather_rows(alpha_below, "pc", n_pc)
    kern, gathered = lax.optimization_barrier((kern, gathered))
    partial_sum = jnp.dot(
        factor_rows,
        gathered,
        precision=lax.Precision.HIGH,
        preferred_element_type=jnp.float32,
    )
    carried = butterfly_sum(partial_sum, "pr", n_pr)
    residual = targets - carried
    alpha_panel = contract_rows(inverse_full, gather_rows(residual, "pc", n_pc))
    update = contract_rows(kern, alpha_panel)
    return predictions_in + update


def solution(mesh):
    placed = (
        P("pr", None),
        P("pc", None),
        P("pc", "pr"),
        P(("pr", "pc"), None),
        P("pc", None),
        P("pc", None),
        P(("pr", "pc"), None),
    )
    return jax.shard_map(
        body, mesh=mesh, in_specs=placed, out_specs=P(("pr", "pc"), None), check_vma=False
    )
```

```python
import math

import jax
import jax.numpy as jnp
from jax import lax
from jax.sharding import PartitionSpec as P

LAYERS = 4


bias_var = 0.1
weight_var = 2.0


ASIN_COEFFS = (4.2163199048e-2, 2.4181311049e-2, 4.5470025998e-2, 7.4953002686e-2, 1.6666752422e-1)


def reflected_arccos(cosine):
    size = jnp.abs(cosine)
    big = size > 0.5
    z = jnp.where(big, 0.5 - 0.5 * size, size * size)
    x = jnp.where(big, jnp.sqrt(z), size)
    poly = ASIN_COEFFS[0]
    for coeff in ASIN_COEFFS[1:]:
        poly = poly * z + coeff
    arcsine = x + x * z * poly
    arccos_size = jnp.where(big, 2.0 * arcsine, 0.5 * math.pi - arcsine)
    return jnp.where(cosine >= 0.0, math.pi - arccos_size, arccos_size)


def arc_kernel(panel, test, test_norms):
    width = panel.shape[1]
    cross = jnp.dot(panel, test.T, preferred_element_type=jnp.float32) / width
    panel_var = jnp.einsum("pd,pd->p", panel, panel, preferred_element_type=jnp.float32) / width
    kern = bias_var + weight_var * cross
    panel_k = bias_var + weight_var * panel_var
    test_k = bias_var + weight_var * (test_norms / width)
    for level in range(LAYERS):
        panel_root = jnp.sqrt(panel_k)
        test_root = jnp.sqrt(test_k)
        spread = panel_root[:, None] * test_root[None, :]
        inverse = (1.0 / panel_root)[:, None] * (1.0 / test_root)[None, :]
        cosine = jnp.clip(kern * inverse, -1.0, 1.0)
        kern = bias_var + weight_var / (2.0 * math.pi) * (
            spread * jnp.sqrt(1.0 - cosine * cosine) + reflected_arccos(cosine) * kern
        )
        panel_k = bias_var + 0.5 * weight_var * panel_k
        test_k = bias_var + 0.5 * weight_var * test_k
    return kern


def contract_rows(left, right):
    return lax.dot_general(
        left,
        right,
        (((0,), (0,)), ((), ())),
        precision=lax.Precision.HIGH,
        preferred_element_type=jnp.float32,
    )


def gather_rows(x, axis, n):
    copies = jnp.broadcast_to(x[None], (n,) + x.shape)
    return lax.all_to_all(copies, axis, 0, 0, tiled=False).reshape((-1,) + x.shape[1:])


def doubling_gather(x, axis, n):
    me = lax.axis_index(axis)
    step = 1
    while step < n:
        upper = (me // step) % 2 == 1
        other = lax.ppermute(x, axis, [(i, i ^ step) for i in range(n)])
        x = jnp.where(upper, jnp.concatenate([other, x]), jnp.concatenate([x, other]))
        step *= 2
    return x


def sum_rows(x, axis, n):
    blocks = lax.all_to_all(x.reshape((n, -1) + x.shape[1:]), axis, 0, 0, tiled=False)
    return gather_rows(blocks.sum(0), axis, n)


def butterfly_sum(x, axis, n):
    step = 1
    while step < n:
        x = x + lax.ppermute(x, axis, [(i, i ^ step) for i in range(n)])
        step *= 2
    return x


def body(
    test_points, panel_points, factor_rows, alpha_below, targets, inverse_block, predictions_in
):
    n_pr = lax.axis_size("pr")
    n_pc = lax.axis_size("pc")
    rows = predictions_in.shape[0]
    own = lax.axis_index("pc")
    panel_all = doubling_gather(panel_points, "pc", n_pc)
    test_own = lax.dynamic_slice_in_dim(test_points, own * rows, rows, 0)
    test_norms = jnp.einsum(
        "nd,nd->n", test_own, test_own, preferred_element_type=jnp.float32
    )
    kern = arc_kernel(panel_all, test_own, test_norms)
    gathered = gather_rows(alpha_below, "pc", n_pc)
    kern, gathered = lax.optimization_barrier((kern, gathered))
    partial_sum = jnp.dot(
        factor_rows,
        gathered,
        precision=lax.Precision.HIGH,
        preferred_element_type=jnp.float32,
    )
    carried = butterfly_sum(partial_sum, "pr", n_pr)
    residual = targets - carried
    alpha_panel = sum_rows(contract_rows(inverse_block, residual), "pc", n_pc)
    update = contract_rows(kern, alpha_panel)
    return predictions_in + update


def solution(mesh):
    placed = (
        P("pr", None),
        P("pc", None),
        P("pc", "pr"),
        P(("pr", "pc"), None),
        P("pc", None),
        P("pc", None),
        P(("pr", "pc"), None),
    )
    return jax.shard_map(
        body, mesh=mesh, in_specs=placed, out_specs=P(("pr", "pc"), None), check_vma=False
    )
```

```python
import math

import jax
import jax.numpy as jnp
from jax import lax
from jax.sharding import PartitionSpec as P

LAYERS = 4


bias_var = 0.1
weight_var = 2.0


ASIN_COEFFS = (4.2163199048e-2, 2.4181311049e-2, 4.5470025998e-2, 7.4953002686e-2, 1.6666752422e-1)


def reflected_arccos(cosine):
    size = jnp.abs(cosine)
    big = size > 0.5
    z = jnp.where(big, 0.5 - 0.5 * size, size * size)
    x = jnp.where(big, jnp.sqrt(z), size)
    poly = ASIN_COEFFS[0]
    for coeff in ASIN_COEFFS[1:]:
        poly = poly * z + coeff
    arcsine = x + x * z * poly
    arccos_size = jnp.where(big, 2.0 * arcsine, 0.5 * math.pi - arcsine)
    return jnp.where(cosine >= 0.0, math.pi - arccos_size, arccos_size)


def arc_kernel(panel, test, test_norms):
    width = panel.shape[1]
    cross = jnp.dot(panel, test.T, preferred_element_type=jnp.float32) / width
    panel_var = jnp.einsum("pd,pd->p", panel, panel, preferred_element_type=jnp.float32) / width
    kern = bias_var + weight_var * cross
    panel_k = bias_var + weight_var * panel_var
    test_k = bias_var + weight_var * (test_norms / width)
    for level in range(LAYERS):
        panel_root = jnp.sqrt(panel_k)
        test_root = jnp.sqrt(test_k)
        spread = panel_root[:, None] * test_root[None, :]
        inverse = (1.0 / panel_root)[:, None] * (1.0 / test_root)[None, :]
        cosine = jnp.clip(kern * inverse, -1.0, 1.0)
        kern = bias_var + weight_var / (2.0 * math.pi) * (
            spread * jnp.sqrt(1.0 - cosine * cosine) + reflected_arccos(cosine) * kern
        )
        panel_k = bias_var + 0.5 * weight_var * panel_k
        test_k = bias_var + 0.5 * weight_var * test_k
    return kern


def contract_rows(left, right):
    return lax.dot_general(
        left,
        right,
        (((0,), (0,)), ((), ())),
        precision=lax.Precision.HIGH,
        preferred_element_type=jnp.float32,
    )


def gather_rows(x, axis, n):
    copies = jnp.broadcast_to(x[None], (n,) + x.shape)
    return lax.all_to_all(copies, axis, 0, 0, tiled=False).reshape((-1,) + x.shape[1:])


def sum_rows(x, axis, n):
    blocks = lax.all_to_all(x.reshape((n, -1) + x.shape[1:]), axis, 0, 0, tiled=False)
    return gather_rows(blocks.sum(0), axis, n)


def butterfly_sum(x, axis, n):
    step = 1
    while step < n:
        x = x + lax.ppermute(x, axis, [(i, i ^ step) for i in range(n)])
        step *= 2
    return x


def body(
    test_points, panel_points, factor_rows, alpha_below, targets, inverse_block, predictions_in
):
    n_pr = lax.axis_size("pr")
    n_pc = lax.axis_size("pc")
    rows = predictions_in.shape[0]
    own = lax.axis_index("pc")
    panel_all = gather_rows(panel_points, "pc", n_pc)
    test_own = lax.dynamic_slice_in_dim(test_points, own * rows, rows, 0)
    test_norms = jnp.einsum(
        "nd,nd->n", test_own, test_own, preferred_element_type=jnp.float32
    )
    kern = arc_kernel(panel_all, test_own, test_norms)
    gathered = gather_rows(alpha_below, "pc", n_pc)
    kern, gathered = lax.optimization_barrier((kern, gathered))
    partial_sum = jnp.dot(
        factor_rows,
        gathered,
        precision=lax.Precision.HIGH,
        preferred_element_type=jnp.float32,
    )
    first_row = lax.axis_index("pr") == 0
    share = jnp.where(first_row, targets, jnp.zeros_like(targets)) - partial_sum
    alpha_panel = sum_rows(contract_rows(inverse_block, share), ("pr", "pc"), n_pr * n_pc)
    update = contract_rows(kern, alpha_panel)
    return predictions_in + update


def solution(mesh):
    placed = (
        P("pr", None),
        P("pc", None),
        P("pc", "pr"),
        P(("pr", "pc"), None),
        P("pc", None),
        P("pc", None),
        P(("pr", "pc"), None),
    )
    return jax.shard_map(
        body, mesh=mesh, in_specs=placed, out_specs=P(("pr", "pc"), None), check_vma=False
    )
```

```python
import math

import jax
import jax.numpy as jnp
from jax import lax
from jax.sharding import PartitionSpec as P

LAYERS = 4


bias_var = 0.1
weight_var = 2.0


ASIN_COEFFS = (4.2163199048e-2, 2.4181311049e-2, 4.5470025998e-2, 7.4953002686e-2, 1.6666752422e-1)


def reflected_arccos(cosine):
    size = jnp.abs(cosine)
    big = size > 0.5
    z = jnp.where(big, 0.5 - 0.5 * size, size * size)
    x = jnp.where(big, jnp.sqrt(z), size)
    poly = ASIN_COEFFS[0]
    for coeff in ASIN_COEFFS[1:]:
        poly = poly * z + coeff
    arcsine = x + x * z * poly
    arccos_size = jnp.where(big, 2.0 * arcsine, 0.5 * math.pi - arcsine)
    return jnp.where(cosine >= 0.0, math.pi - arccos_size, arccos_size)


def arc_kernel(panel, test, test_norms):
    width = panel.shape[1]
    cross = jnp.dot(panel, test.T, preferred_element_type=jnp.float32) / width
    panel_var = jnp.einsum("pd,pd->p", panel, panel, preferred_element_type=jnp.float32) / width
    kern = bias_var + weight_var * cross
    panel_k = bias_var + weight_var * panel_var
    test_k = bias_var + weight_var * (test_norms / width)
    for level in range(LAYERS):
        panel_root = jnp.sqrt(panel_k)
        test_root = jnp.sqrt(test_k)
        spread = panel_root[:, None] * test_root[None, :]
        inverse = (1.0 / panel_root)[:, None] * (1.0 / test_root)[None, :]
        cosine = jnp.clip(kern * inverse, -1.0, 1.0)
        kern = bias_var + weight_var / (2.0 * math.pi) * (
            spread * jnp.sqrt(1.0 - cosine * cosine) + reflected_arccos(cosine) * kern
        )
        panel_k = bias_var + 0.5 * weight_var * panel_k
        test_k = bias_var + 0.5 * weight_var * test_k
    return kern


def contract_rows(left, right):
    return lax.dot_general(
        left,
        right,
        (((0,), (0,)), ((), ())),
        precision=lax.Precision.HIGH,
        preferred_element_type=jnp.float32,
    )


def gather_rows(x, axis, n):
    copies = jnp.broadcast_to(x[None], (n,) + x.shape)
    return lax.all_to_all(copies, axis, 0, 0, tiled=False).reshape((-1,) + x.shape[1:])


def sum_rows(x, axis, n):
    blocks = lax.all_to_all(x.reshape((n, -1) + x.shape[1:]), axis, 0, 0, tiled=False)
    return gather_rows(blocks.sum(0), axis, n)


def butterfly_sum(x, axis, n):
    step = 1
    while step < n:
        x = x + lax.ppermute(x, axis, [(i, i ^ step) for i in range(n)])
        step *= 2
    return x


def body(
    test_points, panel_points, factor_rows, alpha_below, targets, inverse_block, predictions_in
):
    n_pr = lax.axis_size("pr")
    n_pc = lax.axis_size("pc")
    rows = predictions_in.shape[0]
    own = lax.axis_index("pc")
    panel_all = gather_rows(panel_points, "pc", n_pc)
    test_own = lax.dynamic_slice_in_dim(test_points, own * rows, rows, 0)
    test_norms = jnp.einsum(
        "nd,nd->n", test_own, test_own, preferred_element_type=jnp.float32
    )
    split = rows - rows // 8
    kern_a = arc_kernel(panel_all, test_own[:split], test_norms[:split])
    gathered = gather_rows(alpha_below, "pc", n_pc)
    kern_a, gathered = lax.optimization_barrier((kern_a, gathered))
    partial_sum = jnp.dot(
        factor_rows,
        gathered,
        precision=lax.Precision.HIGH,
        preferred_element_type=jnp.float32,
    )
    carried = butterfly_sum(partial_sum, "pr", n_pr)
    residual = targets - carried
    spread_alpha = contract_rows(inverse_block, residual)
    spread_alpha, panel_late = lax.optimization_barrier((spread_alpha, panel_all))
    blocks = lax.all_to_all(
        spread_alpha.reshape((n_pc, -1) + spread_alpha.shape[1:]), "pc", 0, 0, tiled=False
    )
    kern_b = arc_kernel(panel_late, test_own[split:], test_norms[split:])
    kern_b, blocks = lax.optimization_barrier((kern_b, blocks))
    alpha_panel = gather_rows(blocks.sum(0), "pc", n_pc)
    update = contract_rows(jnp.concatenate([kern_a, kern_b], axis=1), alpha_panel)
    return predictions_in + update


def solution(mesh):
    placed = (
        P("pr", None),
        P("pc", None),
        P("pc", "pr"),
        P(("pr", "pc"), None),
        P("pc", None),
        P("pc", None),
        P(("pr", "pc"), None),
    )
    return jax.shard_map(
        body, mesh=mesh, in_specs=placed, out_specs=P(("pr", "pc"), None), check_vma=False
    )
```

```python
import math

import jax
import jax.numpy as jnp
from jax import lax
from jax.sharding import PartitionSpec as P

LAYERS = 4


bias_var = 0.1
weight_var = 2.0


ASIN_COEFFS = (4.2163199048e-2, 2.4181311049e-2, 4.5470025998e-2, 7.4953002686e-2, 1.6666752422e-1)


def reflected_arccos(cosine):
    size = jnp.abs(cosine)
    big = size > 0.5
    z = jnp.where(big, 0.5 - 0.5 * size, size * size)
    x = jnp.where(big, jnp.sqrt(z), size)
    poly = ASIN_COEFFS[0]
    for coeff in ASIN_COEFFS[1:]:
        poly = poly * z + coeff
    arcsine = x + x * z * poly
    arccos_size = jnp.where(big, 2.0 * arcsine, 0.5 * math.pi - arcsine)
    return jnp.where(cosine >= 0.0, math.pi - arccos_size, arccos_size)


def arc_kernel(panel, test, test_norms):
    width = panel.shape[1]
    cross = jnp.dot(panel, test.T, preferred_element_type=jnp.float32) / width
    panel_var = jnp.einsum("pd,pd->p", panel, panel, preferred_element_type=jnp.float32) / width
    kern = bias_var + weight_var * cross
    panel_k = bias_var + weight_var * panel_var
    test_k = bias_var + weight_var * (test_norms / width)
    for level in range(LAYERS):
        panel_root = jnp.sqrt(panel_k)
        test_root = jnp.sqrt(test_k)
        spread = panel_root[:, None] * test_root[None, :]
        inverse = (1.0 / panel_root)[:, None] * (1.0 / test_root)[None, :]
        cosine = jnp.clip(kern * inverse, -1.0, 1.0)
        kern = bias_var + weight_var / (2.0 * math.pi) * (
            spread * jnp.sqrt(1.0 - cosine * cosine) + reflected_arccos(cosine) * kern
        )
        panel_k = bias_var + 0.5 * weight_var * panel_k
        test_k = bias_var + 0.5 * weight_var * test_k
    return kern


def contract_rows(left, right):
    return lax.dot_general(
        left,
        right,
        (((0,), (0,)), ((), ())),
        precision=lax.Precision.HIGH,
        preferred_element_type=jnp.float32,
    )


def gather_rows(x, axis, n):
    copies = jnp.broadcast_to(x[None], (n,) + x.shape)
    return lax.all_to_all(copies, axis, 0, 0, tiled=False).reshape((-1,) + x.shape[1:])


def sum_rows(x, axis, n):
    blocks = lax.all_to_all(x.reshape((n, -1) + x.shape[1:]), axis, 0, 0, tiled=False)
    return gather_rows(blocks.sum(0), axis, n)


def butterfly_sum(x, axis, n):
    step = 1
    while step < n:
        x = x + lax.ppermute(x, axis, [(i, i ^ step) for i in range(n)])
        step *= 2
    return x


def body(
    test_points, panel_points, factor_rows, alpha_below, targets, inverse_block, predictions_in
):
    n_pr = lax.axis_size("pr")
    n_pc = lax.axis_size("pc")
    rows = predictions_in.shape[0]
    own = lax.axis_index("pc")
    panel_all = gather_rows(panel_points, "pc", n_pc)
    test_own = lax.dynamic_slice_in_dim(test_points, own * rows, rows, 0)
    test_norms = jnp.einsum(
        "nd,nd->n", test_own, test_own, preferred_element_type=jnp.float32
    )
    inverse_t = jnp.transpose(inverse_block)
    inverse_t, alpha_below = lax.optimization_barrier((inverse_t, alpha_below))
    split = rows - rows // 8
    kern_a = arc_kernel(panel_all, test_own[:split], test_norms[:split])
    gathered = gather_rows(alpha_below, "pc", n_pc)
    kern_a, gathered = lax.optimization_barrier((kern_a, gathered))
    partial_sum = jnp.dot(
        factor_rows,
        gathered,
        precision=lax.Precision.HIGH,
        preferred_element_type=jnp.float32,
    )
    carried = butterfly_sum(partial_sum, "pr", n_pr)
    residual = targets - carried
    spread_alpha = jnp.dot(
        inverse_t, residual, precision=lax.Precision.HIGH, preferred_element_type=jnp.float32
    )
    spread_alpha, panel_late = lax.optimization_barrier((spread_alpha, panel_all))
    blocks = lax.all_to_all(
        spread_alpha.reshape((n_pc, -1) + spread_alpha.shape[1:]), "pc", 0, 0, tiled=False
    )
    kern_b = arc_kernel(panel_late, test_own[split:], test_norms[split:])
    kern_b, blocks = lax.optimization_barrier((kern_b, blocks))
    alpha_panel = gather_rows(blocks.sum(0), "pc", n_pc)
    update = contract_rows(jnp.concatenate([kern_a, kern_b], axis=1), alpha_panel)
    return predictions_in + update


def solution(mesh):
    placed = (
        P("pr", None),
        P("pc", None),
        P("pc", "pr"),
        P(("pr", "pc"), None),
        P("pc", None),
        P("pc", None),
        P(("pr", "pc"), None),
    )
    return jax.shard_map(
        body, mesh=mesh, in_specs=placed, out_specs=P(("pr", "pc"), None), check_vma=False
    )
```

```python
import math

import jax
import jax.numpy as jnp
from jax import lax
from jax.sharding import PartitionSpec as P

LAYERS = 4


bias_var = 0.1
weight_var = 2.0


ASIN_COEFFS = (4.2163199048e-2, 2.4181311049e-2, 4.5470025998e-2, 7.4953002686e-2, 1.6666752422e-1)


def reflected_arccos(cosine):
    size = jnp.abs(cosine)
    big = size > 0.5
    z = jnp.where(big, 0.5 - 0.5 * size, size * size)
    x = jnp.where(big, jnp.sqrt(z), size)
    poly = ASIN_COEFFS[0]
    for coeff in ASIN_COEFFS[1:]:
        poly = poly * z + coeff
    arcsine = x + x * z * poly
    arccos_size = jnp.where(big, 2.0 * arcsine, 0.5 * math.pi - arcsine)
    return jnp.where(cosine >= 0.0, math.pi - arccos_size, arccos_size)


def arc_kernel(panel, test, test_norms):
    width = panel.shape[1]
    cross = jnp.dot(panel, test.T, preferred_element_type=jnp.float32) / width
    panel_var = jnp.einsum("pd,pd->p", panel, panel, preferred_element_type=jnp.float32) / width
    kern = bias_var + weight_var * cross
    panel_k = bias_var + weight_var * panel_var
    test_k = bias_var + weight_var * (test_norms / width)
    for level in range(LAYERS):
        panel_root = jnp.sqrt(panel_k)
        test_root = jnp.sqrt(test_k)
        spread = panel_root[:, None] * test_root[None, :]
        inverse = (1.0 / panel_root)[:, None] * (1.0 / test_root)[None, :]
        cosine = jnp.clip(kern * inverse, -1.0, 1.0)
        kern = bias_var + weight_var / (2.0 * math.pi) * (
            spread * jnp.sqrt(1.0 - cosine * cosine) + reflected_arccos(cosine) * kern
        )
        panel_k = bias_var + 0.5 * weight_var * panel_k
        test_k = bias_var + 0.5 * weight_var * test_k
    return kern


def contract_rows(left, right):
    return lax.dot_general(
        left,
        right,
        (((0,), (0,)), ((), ())),
        precision=lax.Precision.HIGH,
        preferred_element_type=jnp.float32,
    )


def gather_rows(x, axis, n):
    copies = jnp.broadcast_to(x[None], (n,) + x.shape)
    return lax.all_to_all(copies, axis, 0, 0, tiled=False).reshape((-1,) + x.shape[1:])


def sum_rows(x, axis, n):
    blocks = lax.all_to_all(x.reshape((n, -1) + x.shape[1:]), axis, 0, 0, tiled=False)
    return gather_rows(blocks.sum(0), axis, n)


def butterfly_sum(x, axis, n):
    step = n // 2
    while step >= 1:
        x = x + lax.ppermute(x, axis, [(i, i ^ step) for i in range(n)])
        step //= 2
    return x


def body(
    test_points, panel_points, factor_rows, alpha_below, targets, inverse_block, predictions_in
):
    n_pr = lax.axis_size("pr")
    n_pc = lax.axis_size("pc")
    rows = predictions_in.shape[0]
    own = lax.axis_index("pc")
    panel_all = gather_rows(panel_points, "pc", n_pc)
    test_own = lax.dynamic_slice_in_dim(test_points, own * rows, rows, 0)
    test_norms = jnp.einsum(
        "nd,nd->n", test_own, test_own, preferred_element_type=jnp.float32
    )
    inverse_t = jnp.transpose(inverse_block)
    inverse_t, alpha_below = lax.optimization_barrier((inverse_t, alpha_below))
    split = rows - rows // 8
    kern_a = arc_kernel(panel_all, test_own[:split], test_norms[:split])
    gathered = gather_rows(alpha_below, "pc", n_pc)
    kern_a, gathered = lax.optimization_barrier((kern_a, gathered))
    partial_sum = jnp.dot(
        factor_rows,
        gathered,
        precision=lax.Precision.HIGH,
        preferred_element_type=jnp.float32,
    )
    carried = butterfly_sum(partial_sum, "pr", n_pr)
    residual = targets - carried
    spread_alpha = jnp.dot(
        inverse_t, residual, precision=lax.Precision.HIGH, preferred_element_type=jnp.float32
    )
    spread_alpha, panel_late = lax.optimization_barrier((spread_alpha, panel_all))
    blocks = lax.all_to_all(
        spread_alpha.reshape((n_pc, -1) + spread_alpha.shape[1:]), "pc", 0, 0, tiled=False
    )
    kern_b = arc_kernel(panel_late, test_own[split:], test_norms[split:])
    kern_b, blocks = lax.optimization_barrier((kern_b, blocks))
    alpha_panel = gather_rows(blocks.sum(0), "pc", n_pc)
    update = contract_rows(jnp.concatenate([kern_a, kern_b], axis=1), alpha_panel)
    return predictions_in + update


def solution(mesh):
    placed = (
        P("pr", None),
        P("pc", None),
        P("pc", "pr"),
        P(("pr", "pc"), None),
        P("pc", None),
        P("pc", None),
        P(("pr", "pc"), None),
    )
    return jax.shard_map(
        body, mesh=mesh, in_specs=placed, out_specs=P(("pr", "pc"), None), check_vma=False
    )
```

```python
import math

import jax
import jax.numpy as jnp
from jax import lax
from jax.sharding import PartitionSpec as P

LAYERS = 4


bias_var = 0.1
weight_var = 2.0


ASIN_COEFFS = (4.2163199048e-2, 2.4181311049e-2, 4.5470025998e-2, 7.4953002686e-2, 1.6666752422e-1)


def reflected_arccos(cosine):
    size = jnp.abs(cosine)
    big = size > 0.5
    z = jnp.where(big, 0.5 - 0.5 * size, size * size)
    x = jnp.where(big, jnp.sqrt(z), size)
    poly = ASIN_COEFFS[0]
    for coeff in ASIN_COEFFS[1:]:
        poly = poly * z + coeff
    arcsine = x + x * z * poly
    arccos_size = jnp.where(big, 2.0 * arcsine, 0.5 * math.pi - arcsine)
    return jnp.where(cosine >= 0.0, math.pi - arccos_size, arccos_size)


def arc_kernel(panel, test, test_norms):
    width = panel.shape[1]
    cross = jnp.dot(panel, test.T, preferred_element_type=jnp.float32) / width
    panel_var = jnp.einsum("pd,pd->p", panel, panel, preferred_element_type=jnp.float32) / width
    kern = bias_var + weight_var * cross
    panel_k = bias_var + weight_var * panel_var
    test_k = bias_var + weight_var * (test_norms / width)
    for level in range(LAYERS):
        panel_root = jnp.sqrt(panel_k)
        test_root = jnp.sqrt(test_k)
        spread = panel_root[:, None] * test_root[None, :]
        inverse = (1.0 / panel_root)[:, None] * (1.0 / test_root)[None, :]
        cosine = jnp.clip(kern * inverse, -1.0, 1.0)
        kern = bias_var + weight_var / (2.0 * math.pi) * (
            spread * jnp.sqrt(1.0 - cosine * cosine) + reflected_arccos(cosine) * kern
        )
        panel_k = bias_var + 0.5 * weight_var * panel_k
        test_k = bias_var + 0.5 * weight_var * test_k
    return kern


def contract_rows(left, right):
    return lax.dot_general(
        left,
        right,
        (((0,), (0,)), ((), ())),
        precision=lax.Precision.HIGH,
        preferred_element_type=jnp.float32,
    )


def gather_rows(x, axis, n):
    copies = jnp.broadcast_to(x[None], (n,) + x.shape)
    return lax.all_to_all(copies, axis, 0, 0, tiled=False).reshape((-1,) + x.shape[1:])


def sum_rows(x, axis, n):
    blocks = lax.all_to_all(x.reshape((n, -1) + x.shape[1:]), axis, 0, 0, tiled=False)
    return gather_rows(blocks.sum(0), axis, n)


def butterfly_sum(x, axis, n):
    step = 1
    while step < n:
        x = x + lax.ppermute(x, axis, [(i, i ^ step) for i in range(n)])
        step *= 2
    return x


def body(
    test_points, panel_points, factor_rows, alpha_below, targets, inverse_block, predictions_in
):
    n_pr = lax.axis_size("pr")
    n_pc = lax.axis_size("pc")
    rows = predictions_in.shape[0]
    own = lax.axis_index("pc")
    panel_all = gather_rows(panel_points, "pc", n_pc)
    test_own = lax.dynamic_slice_in_dim(test_points, own * rows, rows, 0)
    test_norms = jnp.einsum(
        "nd,nd->n", test_own, test_own, preferred_element_type=jnp.float32
    )
    inverse_t = jnp.transpose(inverse_block)
    inverse_t, alpha_below = lax.optimization_barrier((inverse_t, alpha_below))
    split = rows - rows // 8
    kern_a = arc_kernel(panel_all, test_own[:split], test_norms[:split])
    high = alpha_below.astype(jnp.bfloat16)
    low = (alpha_below - high.astype(jnp.float32)).astype(jnp.bfloat16)
    gathered = gather_rows(jnp.concatenate([high, low], axis=1), "pc", n_pc)
    kern_a, gathered = lax.optimization_barrier((kern_a, gathered))
    factor_high = factor_rows.astype(jnp.bfloat16)
    factor_low = (factor_rows - factor_high.astype(jnp.float32)).astype(jnp.bfloat16)
    outs = alpha_below.shape[1]
    gathered_high, gathered_low = gathered[:, :outs], gathered[:, outs:]
    partial_sum = (
        jnp.dot(factor_high, gathered_high, preferred_element_type=jnp.float32)
        + jnp.dot(factor_high, gathered_low, preferred_element_type=jnp.float32)
        + jnp.dot(factor_low, gathered_high, preferred_element_type=jnp.float32)
    )
    carried = butterfly_sum(partial_sum, "pr", n_pr)
    residual = targets - carried
    spread_alpha = jnp.dot(
        inverse_t, residual, precision=lax.Precision.HIGH, preferred_element_type=jnp.float32
    )
    spread_alpha, panel_late = lax.optimization_barrier((spread_alpha, panel_all))
    blocks = lax.all_to_all(
        spread_alpha.reshape((n_pc, -1) + spread_alpha.shape[1:]), "pc", 0, 0, tiled=False
    )
    kern_b = arc_kernel(panel_late, test_own[split:], test_norms[split:])
    kern_b, blocks = lax.optimization_barrier((kern_b, blocks))
    alpha_panel = gather_rows(blocks.sum(0), "pc", n_pc)
    update = contract_rows(jnp.concatenate([kern_a, kern_b], axis=1), alpha_panel)
    return predictions_in + update


def solution(mesh):
    placed = (
        P("pr", None),
        P("pc", None),
        P("pc", "pr"),
        P(("pr", "pc"), None),
        P("pc", None),
        P("pc", None),
        P(("pr", "pc"), None),
    )
    return jax.shard_map(
        body, mesh=mesh, in_specs=placed, out_specs=P(("pr", "pc"), None), check_vma=False
    )
```

```python
import math

import jax
import jax.numpy as jnp
from jax import lax
from jax.sharding import PartitionSpec as P

LAYERS = 4


bias_var = 0.1
weight_var = 2.0


ASIN_COEFFS = (4.2163199048e-2, 2.4181311049e-2, 4.5470025998e-2, 7.4953002686e-2, 1.6666752422e-1)


def reflected_arccos(cosine):
    size = jnp.abs(cosine)
    big = size > 0.5
    z = jnp.where(big, 0.5 - 0.5 * size, size * size)
    x = jnp.where(big, jnp.sqrt(z), size)
    poly = ASIN_COEFFS[0]
    for coeff in ASIN_COEFFS[1:]:
        poly = poly * z + coeff
    arcsine = x + x * z * poly
    arccos_size = jnp.where(big, 2.0 * arcsine, 0.5 * math.pi - arcsine)
    return jnp.where(cosine >= 0.0, math.pi - arccos_size, arccos_size)


def arc_kernel(panel, test, test_norms):
    width = panel.shape[1]
    cross = jnp.dot(panel, test.T, preferred_element_type=jnp.float32) / width
    panel_var = jnp.einsum("pd,pd->p", panel, panel, preferred_element_type=jnp.float32) / width
    kern = bias_var + weight_var * cross
    panel_k = bias_var + weight_var * panel_var
    test_k = bias_var + weight_var * (test_norms / width)
    for level in range(LAYERS):
        panel_root = jnp.sqrt(panel_k)
        test_root = jnp.sqrt(test_k)
        spread = panel_root[:, None] * test_root[None, :]
        inverse = (1.0 / panel_root)[:, None] * (1.0 / test_root)[None, :]
        cosine = jnp.clip(kern * inverse, -1.0, 1.0)
        kern = bias_var + weight_var / (2.0 * math.pi) * (
            spread * jnp.sqrt(1.0 - cosine * cosine) + reflected_arccos(cosine) * kern
        )
        panel_k = bias_var + 0.5 * weight_var * panel_k
        test_k = bias_var + 0.5 * weight_var * test_k
    return kern


def contract_rows(left, right):
    return lax.dot_general(
        left,
        right,
        (((0,), (0,)), ((), ())),
        precision=lax.Precision.HIGH,
        preferred_element_type=jnp.float32,
    )


def gather_rows(x, axis, n):
    copies = jnp.broadcast_to(x[None], (n,) + x.shape)
    return lax.all_to_all(copies, axis, 0, 0, tiled=False).reshape((-1,) + x.shape[1:])


def sum_rows(x, axis, n):
    blocks = lax.all_to_all(x.reshape((n, -1) + x.shape[1:]), axis, 0, 0, tiled=False)
    return gather_rows(blocks.sum(0), axis, n)


def butterfly_sum(x, axis, n):
    step = 1
    while step < n:
        x = x + lax.ppermute(x, axis, [(i, i ^ step) for i in range(n)])
        step *= 2
    return x


def body(
    test_points, panel_points, factor_rows, alpha_below, targets, inverse_block, predictions_in
):
    n_pr = lax.axis_size("pr")
    n_pc = lax.axis_size("pc")
    rows = predictions_in.shape[0]
    own = lax.axis_index("pc")
    panel_all = gather_rows(panel_points, "pc", n_pc)
    test_own = lax.dynamic_slice_in_dim(test_points, own * rows, rows, 0)
    test_norms = jnp.einsum(
        "nd,nd->n", test_own, test_own, preferred_element_type=jnp.float32
    )
    inverse_t = jnp.transpose(inverse_block)
    inverse_t, alpha_below = lax.optimization_barrier((inverse_t, alpha_below))
    split = rows - rows // 8
    kern_a = arc_kernel(panel_all, test_own[:split], test_norms[:split])
    gathered = gather_rows(alpha_below, "pc", n_pc)
    kern_a, gathered = lax.optimization_barrier((kern_a, gathered))
    partial_sum = jnp.dot(
        factor_rows,
        gathered,
        precision=lax.Precision.HIGH,
        preferred_element_type=jnp.float32,
    )
    carried = butterfly_sum(partial_sum, "pr", n_pr)
    residual = targets - carried
    spread_alpha = jnp.dot(
        inverse_t, residual, precision=lax.Precision.HIGH, preferred_element_type=jnp.float32
    )
    spread_alpha, panel_late = lax.optimization_barrier((spread_alpha, panel_all))
    blocks = lax.all_to_all(
        spread_alpha.reshape((n_pc, -1) + spread_alpha.shape[1:]), "pc", 0, 0, tiled=False
    )
    own_block = blocks.sum(0)
    own_block, panel_late = lax.optimization_barrier((own_block, panel_late))
    alpha_panel = gather_rows(own_block, "pc", n_pc)
    kern_b = arc_kernel(panel_late, test_own[split:], test_norms[split:])
    kern_b, alpha_panel = lax.optimization_barrier((kern_b, alpha_panel))
    update = contract_rows(jnp.concatenate([kern_a, kern_b], axis=1), alpha_panel)
    return predictions_in + update


def solution(mesh):
    placed = (
        P("pr", None),
        P("pc", None),
        P("pc", "pr"),
        P(("pr", "pc"), None),
        P("pc", None),
        P("pc", None),
        P(("pr", "pc"), None),
    )
    return jax.shard_map(
        body, mesh=mesh, in_specs=placed, out_specs=P(("pr", "pc"), None), check_vma=False
    )
```

```python
import math

import jax
import jax.numpy as jnp
from jax import lax
from jax.sharding import PartitionSpec as P

LAYERS = 4


bias_var = 0.1
weight_var = 2.0


ASIN_COEFFS = (4.2163199048e-2, 2.4181311049e-2, 4.5470025998e-2, 7.4953002686e-2, 1.6666752422e-1)


def reflected_arccos(cosine):
    size = jnp.abs(cosine)
    big = size > 0.5
    z = jnp.where(big, 0.5 - 0.5 * size, size * size)
    x = jnp.where(big, jnp.sqrt(z), size)
    poly = ASIN_COEFFS[0]
    for coeff in ASIN_COEFFS[1:]:
        poly = poly * z + coeff
    arcsine = x + x * z * poly
    arccos_size = jnp.where(big, 2.0 * arcsine, 0.5 * math.pi - arcsine)
    return jnp.where(cosine >= 0.0, math.pi - arccos_size, arccos_size)


def arc_kernel(panel, test, test_norms):
    width = panel.shape[1]
    cross = jnp.dot(panel, test.T, preferred_element_type=jnp.float32) / width
    panel_var = jnp.einsum("pd,pd->p", panel, panel, preferred_element_type=jnp.float32) / width
    kern = bias_var + weight_var * cross
    panel_k = bias_var + weight_var * panel_var
    test_k = bias_var + weight_var * (test_norms / width)
    for level in range(LAYERS):
        panel_root = jnp.sqrt(panel_k)
        test_root = jnp.sqrt(test_k)
        spread = panel_root[:, None] * test_root[None, :]
        inverse = (1.0 / panel_root)[:, None] * (1.0 / test_root)[None, :]
        cosine = jnp.clip(kern * inverse, -1.0, 1.0)
        kern = bias_var + weight_var / (2.0 * math.pi) * (
            spread * jnp.sqrt(1.0 - cosine * cosine) + reflected_arccos(cosine) * kern
        )
        panel_k = bias_var + 0.5 * weight_var * panel_k
        test_k = bias_var + 0.5 * weight_var * test_k
    return kern


def contract_rows(left, right):
    return lax.dot_general(
        left,
        right,
        (((0,), (0,)), ((), ())),
        precision=lax.Precision.HIGH,
        preferred_element_type=jnp.float32,
    )


def gather_rows(x, axis, n):
    copies = jnp.broadcast_to(x[None], (n,) + x.shape)
    return lax.all_to_all(copies, axis, 0, 0, tiled=False).reshape((-1,) + x.shape[1:])


def sum_rows(x, axis, n):
    blocks = lax.all_to_all(x.reshape((n, -1) + x.shape[1:]), axis, 0, 0, tiled=False)
    return gather_rows(blocks.sum(0), axis, n)


def butterfly_sum(x, axis, n):
    step = 1
    while step < n:
        x = x + lax.ppermute(x, axis, [(i, i ^ step) for i in range(n)])
        step *= 2
    return x


def body(
    test_points, panel_points, factor_rows, alpha_below, targets, inverse_block, predictions_in
):
    n_pr = lax.axis_size("pr")
    n_pc = lax.axis_size("pc")
    rows = predictions_in.shape[0]
    own = lax.axis_index("pc")
    panel_all = gather_rows(panel_points, "pc", n_pc)
    test_own = lax.dynamic_slice_in_dim(test_points, own * rows, rows, 0)
    test_norms = jnp.einsum(
        "nd,nd->n", test_own, test_own, preferred_element_type=jnp.float32
    )
    inverse_t = jnp.transpose(inverse_block)
    inverse_t, alpha_below = lax.optimization_barrier((inverse_t, alpha_below))
    split = rows - 3 * rows // 16
    kern_a = arc_kernel(panel_all, test_own[:split], test_norms[:split])
    gathered = gather_rows(alpha_below, "pc", n_pc)
    kern_a, gathered = lax.optimization_barrier((kern_a, gathered))
    partial_sum = jnp.dot(
        factor_rows,
        gathered,
        precision=lax.Precision.HIGH,
        preferred_element_type=jnp.float32,
    )
    carried = butterfly_sum(partial_sum, "pr", n_pr)
    residual = targets - carried
    spread_alpha = jnp.dot(
        inverse_t, residual, precision=lax.Precision.HIGH, preferred_element_type=jnp.float32
    )
    spread_alpha, panel_late = lax.optimization_barrier((spread_alpha, panel_all))
    blocks = lax.all_to_all(
        spread_alpha.reshape((n_pc, -1) + spread_alpha.shape[1:]), "pc", 0, 0, tiled=False
    )
    kern_b = arc_kernel(panel_late, test_own[split:], test_norms[split:])
    kern_b, blocks = lax.optimization_barrier((kern_b, blocks))
    alpha_panel = gather_rows(blocks.sum(0), "pc", n_pc)
    update = contract_rows(jnp.concatenate([kern_a, kern_b], axis=1), alpha_panel)
    return predictions_in + update


def solution(mesh):
    placed = (
        P("pr", None),
        P("pc", None),
        P("pc", "pr"),
        P(("pr", "pc"), None),
        P("pc", None),
        P("pc", None),
        P(("pr", "pc"), None),
    )
    return jax.shard_map(
        body, mesh=mesh, in_specs=placed, out_specs=P(("pr", "pc"), None), check_vma=False
    )
```

```python
import math

import jax
import jax.numpy as jnp
from jax import lax
from jax.sharding import PartitionSpec as P

LAYERS = 4


bias_var = 0.1
weight_var = 2.0


ASIN_COEFFS = (4.2163199048e-2, 2.4181311049e-2, 4.5470025998e-2, 7.4953002686e-2, 1.6666752422e-1)


def reflected_arccos(cosine):
    size = jnp.abs(cosine)
    big = size > 0.5
    z = jnp.where(big, 0.5 - 0.5 * size, size * size)
    x = jnp.where(big, jnp.sqrt(z), size)
    poly = ASIN_COEFFS[0]
    for coeff in ASIN_COEFFS[1:]:
        poly = poly * z + coeff
    arcsine = x + x * z * poly
    arccos_size = jnp.where(big, 2.0 * arcsine, 0.5 * math.pi - arcsine)
    return jnp.where(cosine >= 0.0, math.pi - arccos_size, arccos_size)


def arc_kernel(panel, test, test_norms):
    width = panel.shape[1]
    cross = jnp.dot(panel, test.T, preferred_element_type=jnp.float32) / width
    panel_var = jnp.einsum("pd,pd->p", panel, panel, preferred_element_type=jnp.float32) / width
    kern = bias_var + weight_var * cross
    panel_k = bias_var + weight_var * panel_var
    test_k = bias_var + weight_var * (test_norms / width)
    for level in range(LAYERS):
        panel_root = jnp.sqrt(panel_k)
        test_root = jnp.sqrt(test_k)
        spread = panel_root[:, None] * test_root[None, :]
        inverse = (1.0 / panel_root)[:, None] * (1.0 / test_root)[None, :]
        cosine = jnp.clip(kern * inverse, -1.0, 1.0)
        kern = bias_var + weight_var / (2.0 * math.pi) * (
            spread * jnp.sqrt(1.0 - cosine * cosine) + reflected_arccos(cosine) * kern
        )
        panel_k = bias_var + 0.5 * weight_var * panel_k
        test_k = bias_var + 0.5 * weight_var * test_k
    return kern


def contract_rows(left, right):
    return lax.dot_general(
        left,
        right,
        (((0,), (0,)), ((), ())),
        precision=lax.Precision.HIGH,
        preferred_element_type=jnp.float32,
    )


def gather_rows(x, axis, n):
    copies = jnp.broadcast_to(x[None], (n,) + x.shape)
    return lax.all_to_all(copies, axis, 0, 0, tiled=False).reshape((-1,) + x.shape[1:])


def sum_rows(x, axis, n):
    blocks = lax.all_to_all(x.reshape((n, -1) + x.shape[1:]), axis, 0, 0, tiled=False)
    return gather_rows(blocks.sum(0), axis, n)


def butterfly_sum(x, axis, n):
    step = 1
    while step < n:
        x = x + lax.ppermute(x, axis, [(i, i ^ step) for i in range(n)])
        step *= 2
    return x


def body(
    test_points, panel_points, factor_rows, alpha_below, targets, inverse_block, predictions_in
):
    n_pr = lax.axis_size("pr")
    n_pc = lax.axis_size("pc")
    rows = predictions_in.shape[0]
    own = lax.axis_index("pc")
    panel_all = gather_rows(panel_points, "pc", n_pc)
    test_own = lax.dynamic_slice_in_dim(test_points, own * rows, rows, 0)
    test_norms = jnp.einsum(
        "nd,nd->n", test_own, test_own, preferred_element_type=jnp.float32
    )
    inverse_t = jnp.transpose(inverse_block)
    inverse_t, alpha_below = lax.optimization_barrier((inverse_t, alpha_below))
    split = rows - rows // 4
    kern_a = arc_kernel(panel_all, test_own[:split], test_norms[:split])
    gathered = gather_rows(alpha_below, "pc", n_pc)
    kern_a, gathered = lax.optimization_barrier((kern_a, gathered))
    partial_sum = jnp.dot(
        factor_rows,
        gathered,
        precision=lax.Precision.HIGH,
        preferred_element_type=jnp.float32,
    )
    carried = butterfly_sum(partial_sum, "pr", n_pr)
    residual = targets - carried
    spread_alpha = jnp.dot(
        inverse_t, residual, precision=lax.Precision.HIGH, preferred_element_type=jnp.float32
    )
    spread_alpha, panel_late = lax.optimization_barrier((spread_alpha, panel_all))
    blocks = lax.all_to_all(
        spread_alpha.reshape((n_pc, -1) + spread_alpha.shape[1:]), "pc", 0, 0, tiled=False
    )
    kern_b = arc_kernel(panel_late, test_own[split:], test_norms[split:])
    kern_b, blocks = lax.optimization_barrier((kern_b, blocks))
    alpha_panel = gather_rows(blocks.sum(0), "pc", n_pc)
    update = contract_rows(jnp.concatenate([kern_a, kern_b], axis=1), alpha_panel)
    return predictions_in + update


def solution(mesh):
    placed = (
        P("pr", None),
        P("pc", None),
        P("pc", "pr"),
        P(("pr", "pc"), None),
        P("pc", None),
        P("pc", None),
        P(("pr", "pc"), None),
    )
    return jax.shard_map(
        body, mesh=mesh, in_specs=placed, out_specs=P(("pr", "pc"), None), check_vma=False
    )
```
